256 devices in a mesh: grp: 32 (over x, z), shard: 8 (over y, core).
Axes of the slice: x: 4, y: 4, z: 8, core: 2. Of those that a mesh axis runs over, the one named last changes fastest.
Arguments:
- layer_inputs: bfloat16 [131072, 1600], P(('grp', 'shard')), may hold values from -6 to 6
- cotangents: bfloat16 [131072, 1600], P(('grp', 'shard')), may hold values from -0.25 to 0.25
- weight: bfloat16 [1600, 1600], P('shard'), may hold values from -0.15625 to 0.15625
- error_state: float32 [32, 1600, 1600], P('grp', 'shard'), may hold values from -6 to 6
- momentum: float32 [1600, 1600], P('shard'), may hold values from -0.75 to 0.75
- bias_momentum: float32 [1600], replicated, may hold values from -6 to 6
- start_basis: float32 [1600, 32], replicated, may hold values from -6 to 6
- next_inputs: bfloat16 [131072, 1600], P(('grp', 'shard')), may hold values from -6 to 6
Outputs:
- next_outputs: bfloat16 [131072, 1600], P(('grp', 'shard'))
- new_error: float32 [32, 1600, 1600], P('grp', 'shard')
- new_momentum: float32 [1600, 1600], P('shard')
- new_bias_momentum: float32 [1600], replicated
The draws below stay inside these ranges and needn't reach their ends.
All inputs are finite; a program needn't handle non-finite values.
Results may differ from the reference program's by a relative error of at most 0.015.
Values may be sent and summed in bfloat16 or wider, within the bound.
No kernel may reach another device: no remote copies, remote signals or barrier semaphores. Data moves between devices by JAX's collectives and lax.ppermute only.
A program may use at most 128 MiB of HBM per device.

```python
import jax
import jax.numpy as jnp
from jax import lax

D = 1600
RANK = 32
GROUP_TOK = 4096
TOKENS = 131072
N_GRP = 32


def strengthened(array, key, source, target, shards_of, factor):
    def block_of(axis_at):
        return (jnp.arange(array.shape[axis_at]) // (array.shape[axis_at] // shards_of)).reshape((-1,) + (1,) * (array.ndim - 1 - axis_at))

    first = jax.random.permutation(key, shards_of)[block_of(target)]
    second = (block_of(target) + shards_of // 2) % shards_of
    return jnp.where((block_of(source) == first) | (block_of(source) == second), factor * array, array)


def levels(rng, extent, cuts, low, top_value):
    factor_of = 1.0
    for dim, blocks in cuts:
        draws = jax.random.uniform(jax.random.fold_in(jax.random.fold_in(rng, 6), dim), (blocks,), jnp.float32, low / len(cuts), top_value / len(cuts))
        factor_of = factor_of * jnp.repeat(jnp.exp(draws), extent[dim] // blocks).reshape((-1,) + (1,) * (len(extent) - 1 - dim))
    return factor_of


def normal_values(stream_key, dims, width, limit, shards=(), held_as=jnp.bfloat16):
    loudness = levels(stream_key, dims, shards, -0.22, 0.18) if shards else 1.0
    drawn = jax.random.normal(stream_key, dims, jnp.float32) * width * loudness
    return jnp.minimum(jnp.maximum(drawn, -limit), limit).astype(held_as)


def bell_draw_with(own_key, shape, scale, reach, shards, heavy, kind=jnp.bfloat16):
    array = scale * jax.random.normal(own_key, shape, jnp.float32)
    if shards:
        array = array * levels(own_key, shape, shards, -0.22, 0.18)
    return jnp.clip(strengthened(array, jax.random.fold_in(own_key, 3), *heavy), -reach, reach).astype(kind)


def setup_inputs(seed: int = 0) -> dict:
    splits = jax.random.split(jax.random.key(seed), 9)
    layer_inputs = normal_values(splits[0], (TOKENS, D), 1.0, 6.0, ((0, 256),))
    cotangents = bell_draw_with(splits[1], (TOKENS, D), GROUP_TOK ** -0.5, 0.25, ((0, 256),), (0, 1, 64, 4.0))
    weight = normal_values(splits[2], (D, D), D ** -0.5, 0.15625, ((0, 8),))
    error_state = normal_values(splits[3], (N_GRP, D, D), 0.5, 6.0, ((0, 32), (1, 8)), jnp.float32)
    momentum = normal_values(splits[4], (D, D), 0.05, 0.75, ((0, 8),), jnp.float32)
    bias_momentum = normal_values(splits[5], (D,), 0.5, 6.0, (), jnp.float32)
    start_basis = normal_values(splits[6], (D, RANK), 1.0, 6.0, (), jnp.float32)
    next_inputs = normal_values(splits[7], (TOKENS, D), 1.0, 6.0, ((0, 256),))
    return {"layer_inputs": layer_inputs, "cotangents": cotangents, "weight": weight, "error_state": error_state, "momentum": momentum, "bias_momentum": bias_momentum, "start_basis": start_basis, "next_inputs": next_inputs}


momentum_decay = 0.9
learn_rate = 0.1

def group_gradient(pair):
    inputs_block, cotan_block = pair
    return jnp.dot(inputs_block.T.astype(jnp.float32), cotan_block.astype(jnp.float32), preferred_element_type=jnp.float32)

def reference(layer_inputs, cotangents, weight, error_state, momentum, bias_momentum, start_basis, next_inputs):
    inputs_grouped = layer_inputs.reshape(N_GRP, GROUP_TOK, D)
    cotan_grouped = cotangents.reshape(N_GRP, GROUP_TOK, D)
    gradients = lax.map(group_gradient, (inputs_grouped, cotan_grouped))
    corrected = gradients + error_state
    total = jnp.sum(corrected, axis=0)
    bias_grad = jnp.sum(cotangents, axis=0, dtype=jnp.float32) / N_GRP
    highest = lax.Precision.HIGHEST
    basis = start_basis
    ortho = start_basis
    for round_index in range(2):
        factor = jnp.dot(total, basis, precision=highest)
        gram = jnp.dot(factor.T, factor, precision=highest)
        lower_factor = jnp.linalg.cholesky(gram)
        ortho = jax.scipy.linalg.solve_triangular(lower_factor, factor.T, lower=True).T
        basis = jnp.dot(total.T, ortho, precision=highest) / N_GRP
    approx = jnp.dot(ortho, basis.T, precision=highest)
    new_error = corrected - approx[None, :, :]
    new_momentum = momentum_decay * momentum + approx
    new_bias_momentum = momentum_decay * bias_momentum + bias_grad
    new_weight = (weight.astype(jnp.float32) - learn_rate * new_momentum).astype(jnp.bfloat16)
    next_outputs = jnp.dot(next_inputs.astype(jnp.float32), new_weight.astype(jnp.float32), preferred_element_type=jnp.float32).astype(jnp.bfloat16)
    return (next_outputs, new_error, new_momentum, new_bias_momentum)
```

```python
import jax
import jax.numpy as jnp
from jax import lax
from jax.sharding import PartitionSpec as P

momentum_decay = 0.9
learn_rate = 0.1


def shards(
    layer_inputs, cotangents, weight, error_state, momentum, bias_momentum, start_basis, next_inputs
):
    highest = lax.Precision.HIGHEST
    group_count = lax.axis_size("grp")
    rank = start_basis.shape[1]
    gradient = lax.psum_scatter(
        lax.dot_general(
            layer_inputs, cotangents, (((0,), (0,)), ((), ())), preferred_element_type=jnp.float32
        ).astype(jnp.bfloat16),
        "shard",
        scatter_dimension=0,
        tiled=True,
    ).astype(jnp.float32)
    column_sums = jnp.sum(cotangents, axis=0, dtype=jnp.float32)
    corrected = gradient + error_state[0]
    summed = lax.psum(jnp.concatenate([corrected, column_sums[None, :]], axis=0), "grp")
    total = summed[:-1]
    grp_sums = summed[-1]
    basis = start_basis
    ortho = start_basis
    for round_index in range(2):
        factor = jnp.dot(total, basis, precision=highest)
        gram_part = jnp.dot(factor.T, factor, precision=highest)
        if round_index == 0:
            packed = lax.psum(jnp.concatenate([gram_part.reshape(-1), grp_sums]), "shard")
            gram = packed[: rank * rank].reshape(rank, rank)
            all_sums = packed[rank * rank :]
        else:
            gram = lax.psum(gram_part, "shard")
        lower_factor = jnp.linalg.cholesky(gram)
        ortho = jax.scipy.linalg.solve_triangular(lower_factor, factor.T, lower=True).T
        partial_basis = lax.dot_general(
            total, ortho, (((0,), (0,)), ((), ())), precision=highest
        )
        basis = lax.psum(partial_basis, "shard") / group_count
    approx = jnp.dot(ortho, basis.T, precision=highest)
    new_error = (corrected - approx)[None, :, :]
    new_momentum = momentum_decay * momentum + approx
    new_bias_momentum = momentum_decay * bias_momentum + all_sums / group_count
    new_weight = (weight.astype(jnp.float32) - learn_rate * new_momentum).astype(jnp.bfloat16)
    projected = jnp.dot(
        next_inputs,
        lax.all_gather(new_weight, "shard", axis=0, tiled=True),
        preferred_element_type=jnp.float32,
    )
    return (projected.astype(jnp.bfloat16), new_error, new_momentum, new_bias_momentum)


def solution(mesh):
    placed = (
        P(("grp", "shard"), None),
        P(("grp", "shard"), None),
        P("shard", None),
        P("grp", "shard", None),
        P("shard", None),
        P(),
        P(),
        P(("grp", "shard"), None),
    )
    return jax.shard_map(
        shards,
        mesh=mesh,
        in_specs=placed,
        out_specs=(P(("grp", "shard"), None), P("grp", "shard", None), P("shard", None), P()),
        check_vma=False,
    )
```

```python
import jax
import jax.numpy as jnp
from jax import lax
from jax.sharding import PartitionSpec as P

momentum_decay = 0.9
learn_rate = 0.1


def shards(
    layer_inputs, cotangents, weight, error_state, momentum, bias_momentum, start_basis, next_inputs
):
    highest = lax.Precision.HIGHEST
    group_count = lax.axis_size("grp")
    shard_count = lax.axis_size("shard")
    gradient = lax.psum_scatter(
        lax.dot_general(
            layer_inputs, cotangents, (((0,), (0,)), ((), ())), preferred_element_type=jnp.float32
        ).astype(jnp.bfloat16),
        "shard",
        scatter_dimension=0,
        tiled=True,
    ).astype(jnp.float32)
    column_sums = jnp.sum(cotangents, axis=0, dtype=jnp.float32)
    corrected = gradient + error_state[0]
    own_rows = corrected.shape[0]
    block = own_rows + 1
    summed = lax.psum(jnp.concatenate([corrected, column_sums[None, :]], axis=0), "grp")
    extended = lax.all_gather(summed, "shard", axis=0, tiled=True)
    all_sums = jnp.sum(extended.reshape(shard_count, block, -1)[:, own_rows], axis=0)
    is_total_row = (jnp.arange(shard_count * block) % block < own_rows)[:, None]
    basis = start_basis
    ortho = start_basis
    for round_index in range(2):
        factor = jnp.where(is_total_row, jnp.dot(extended, basis, precision=highest), 0.0)
        gram = jnp.dot(factor.T, factor, precision=highest)
        lower_factor = jnp.linalg.cholesky(gram)
        ortho = jax.scipy.linalg.solve_triangular(lower_factor, factor.T, lower=True).T
        basis = (
            lax.dot_general(extended, ortho, (((0,), (0,)), ((), ())), precision=highest)
            / group_count
        )
    own_ortho = lax.dynamic_slice_in_dim(ortho, lax.axis_index("shard") * block, own_rows, axis=0)
    approx = jnp.dot(own_ortho, basis.T, precision=highest)
    new_error = (corrected - approx)[None, :, :]
    new_momentum = momentum_decay * momentum + approx
    new_bias_momentum = momentum_decay * bias_momentum + all_sums / group_count
    new_weight = (weight.astype(jnp.float32) - learn_rate * new_momentum).astype(jnp.bfloat16)
    projected = jnp.dot(
        next_inputs,
        lax.all_gather(new_weight, "shard", axis=0, tiled=True),
        preferred_element_type=jnp.float32,
    )
    return (projected.astype(jnp.bfloat16), new_error, new_momentum, new_bias_momentum)


def solution(mesh):
    placed = (
        P(("grp", "shard"), None),
        P(("grp", "shard"), None),
        P("shard", None),
        P("grp", "shard", None),
        P("shard", None),
        P(),
        P(),
        P(("grp", "shard"), None),
    )
    return jax.shard_map(
        shards,
        mesh=mesh,
        in_specs=placed,
        out_specs=(P(("grp", "shard"), None), P("grp", "shard", None), P("shard", None), P()),
        check_vma=False,
    )
```

```python
import jax
import jax.numpy as jnp
from jax import lax
from jax.sharding import PartitionSpec as P

momentum_decay = 0.9
learn_rate = 0.1


def shards(
    layer_inputs, cotangents, weight, error_state, momentum, bias_momentum, start_basis, next_inputs
):
    highest = lax.Precision.HIGHEST
    high = lax.Precision.HIGH
    group_count = lax.axis_size("grp")
    shard_count = lax.axis_size("shard")
    gradient = lax.psum_scatter(
        lax.dot_general(
            layer_inputs, cotangents, (((0,), (0,)), ((), ())), preferred_element_type=jnp.float32
        ).astype(jnp.bfloat16),
        "shard",
        scatter_dimension=0,
        tiled=True,
    ).astype(jnp.float32)
    column_sums = jnp.sum(cotangents, axis=0, dtype=jnp.float32)
    corrected = gradient + error_state[0]
    own_rows = corrected.shape[0]
    block = own_rows + 8
    padding = jnp.zeros((block - own_rows - 1, corrected.shape[1]), jnp.float32)
    summed = lax.psum(jnp.concatenate([corrected, column_sums[None, :], padding], axis=0), "grp")
    extended = lax.all_gather(summed, "shard", axis=0, tiled=True)
    all_sums = jnp.sum(extended.reshape(shard_count, block, -1)[:, own_rows], axis=0)
    is_total_row = (jnp.arange(shard_count * block) % block < own_rows)[:, None]
    basis = start_basis
    ortho = start_basis
    for round_index in range(2):
        factor = jnp.where(is_total_row, jnp.dot(extended, basis, precision=high), 0.0)
        gram = jnp.dot(factor.T, factor, precision=highest)
        lower_factor = jnp.linalg.cholesky(gram)
        ortho = jax.scipy.linalg.solve_triangular(lower_factor, factor.T, lower=True).T
        basis = (
            lax.dot_general(extended, ortho, (((0,), (0,)), ((), ())), precision=high)
            / group_count
        )
    own_ortho = lax.dynamic_slice_in_dim(ortho, lax.axis_index("shard") * block, own_rows, axis=0)
    approx = jnp.dot(own_ortho, basis.T, precision=highest)
    new_error = (corrected - approx)[None, :, :]
    new_momentum = momentum_decay * momentum + approx
    new_bias_momentum = momentum_decay * bias_momentum + all_sums / group_count
    new_weight = (weight.astype(jnp.float32) - learn_rate * new_momentum).astype(jnp.bfloat16)
    projected = jnp.dot(
        next_inputs,
        lax.all_gather(new_weight, "shard", axis=0, tiled=True),
        preferred_element_type=jnp.float32,
    )
    return (projected.astype(jnp.bfloat16), new_error, new_momentum, new_bias_momentum)


def solution(mesh):
    placed = (
        P(("grp", "shard"), None),
        P(("grp", "shard"), None),
        P("shard", None),
        P("grp", "shard", None),
        P("shard", None),
        P(),
        P(),
        P(("grp", "shard"), None),
    )
    return jax.shard_map(
        shards,
        mesh=mesh,
        in_specs=placed,
        out_specs=(P(("grp", "shard"), None), P("grp", "shard", None), P("shard", None), P()),
        check_vma=False,
    )
```

```python
import jax
import jax.numpy as jnp
from jax import lax
from jax.sharding import Mesh, PartitionSpec as P

momentum_decay = 0.9
learn_rate = 0.1


def shards(
    layer_inputs, cotangents, weight, error_state, momentum, bias_momentum, start_basis, next_inputs
):
    highest = lax.Precision.HIGHEST
    high = lax.Precision.HIGH
    group_count = lax.axis_size("gx") * lax.axis_size("gz")
    shard_count = lax.axis_size("shard")
    gradient = lax.psum_scatter(
        lax.dot_general(
            layer_inputs, cotangents, (((0,), (0,)), ((), ())), preferred_element_type=jnp.float32
        ).astype(jnp.bfloat16),
        "shard",
        scatter_dimension=0,
        tiled=True,
    ).astype(jnp.float32)
    column_sums = jnp.sum(cotangents, axis=0, dtype=jnp.float32)
    corrected = gradient + error_state[0]
    own_rows = corrected.shape[0]
    block = own_rows + 8
    padding = jnp.zeros((block - own_rows - 1, corrected.shape[1]), jnp.float32)
    summed = lax.psum(
        lax.psum(jnp.concatenate([corrected, column_sums[None, :], padding], axis=0), "gz"), "gx"
    )
    extended = lax.all_gather(summed, "shard", axis=0, tiled=True)
    all_sums = jnp.sum(extended.reshape(shard_count, block, -1)[:, own_rows], axis=0)
    is_total_row = (jnp.arange(shard_count * block) % block < own_rows)[:, None]
    basis = start_basis
    ortho = start_basis
    for round_index in range(2):
        factor = jnp.where(is_total_row, jnp.dot(extended, basis, precision=high), 0.0)
        gram = jnp.dot(factor.T, factor, precision=highest)
        lower_factor = jnp.linalg.cholesky(gram)
        ortho = jax.scipy.linalg.solve_triangular(lower_factor, factor.T, lower=True).T
        basis = (
            lax.dot_general(extended, ortho, (((0,), (0,)), ((), ())), precision=high)
            / group_count
        )
    own_ortho = lax.dynamic_slice_in_dim(ortho, lax.axis_index("shard") * block, own_rows, axis=0)
    approx = jnp.dot(own_ortho, basis.T, precision=highest)
    new_error = (corrected - approx)[None, :, :]
    new_momentum = momentum_decay * momentum + approx
    new_bias_momentum = momentum_decay * bias_momentum + all_sums / group_count
    new_weight = (weight.astype(jnp.float32) - learn_rate * new_momentum).astype(jnp.bfloat16)
    projected = jnp.dot(
        next_inputs,
        lax.all_gather(new_weight, "shard", axis=0, tiled=True),
        preferred_element_type=jnp.float32,
    )
    return (projected.astype(jnp.bfloat16), new_error, new_momentum, new_bias_momentum)


def split_grp(mesh):
    devices = mesh.devices
    x_count = len({device.coords[0] for device in devices[:, 0]})
    shape = (x_count, devices.shape[0] // x_count, devices.shape[1])
    return Mesh(devices.reshape(shape), ("gx", "gz", "shard"))


def solution(mesh):
    grp = ("gx", "gz")
    placed = (
        P((*grp, "shard"), None),
        P((*grp, "shard"), None),
        P("shard", None),
        P(grp, "shard", None),
        P("shard", None),
        P(),
        P(),
        P((*grp, "shard"), None),
    )
    return jax.shard_map(
        shards,
        mesh=split_grp(mesh),
        in_specs=placed,
        out_specs=(P((*grp, "shard"), None), P(grp, "shard", None), P("shard", None), P()),
        check_vma=False,
    )
```

```python
import jax
import jax.numpy as jnp
from jax import lax
from jax.sharding import Mesh, PartitionSpec as P

momentum_decay = 0.9
learn_rate = 0.1


def shards(
    layer_inputs, cotangents, weight, error_state, momentum, bias_momentum, start_basis, next_inputs
):
    highest = lax.Precision.HIGHEST
    rank = start_basis.shape[1]
    group_count = lax.axis_size("gx") * lax.axis_size("gz")
    shard_count = lax.axis_size("shard")
    gradient = lax.psum_scatter(
        lax.dot_general(
            layer_inputs, cotangents, (((0,), (0,)), ((), ())), preferred_element_type=jnp.float32
        ).astype(jnp.bfloat16),
        "shard",
        scatter_dimension=0,
        tiled=True,
    ).astype(jnp.float32)
    column_sums = jnp.sum(cotangents, axis=0, dtype=jnp.float32)
    corrected = gradient + error_state[0]
    own_rows = corrected.shape[0]
    block = own_rows + 8
    padding = jnp.zeros((block - own_rows - 1, corrected.shape[1]), jnp.float32)
    summed = lax.psum(
        lax.psum(jnp.concatenate([corrected, column_sums[None, :], padding], axis=0), "gz"), "gx"
    )
    high_part = summed.astype(jnp.bfloat16)
    low_part = (summed - high_part.astype(jnp.float32)).astype(jnp.bfloat16)
    gathered = lax.all_gather(
        jnp.concatenate([high_part, low_part], axis=0), "shard", axis=0, tiled=True
    )
    split_rows = gathered.reshape(shard_count, 2, block, -1)
    sum_rows = split_rows[:, :, own_rows].astype(jnp.float32)
    all_sums = jnp.sum(sum_rows[:, 0] + sum_rows[:, 1], axis=0)
    is_total_row = (jnp.arange(shard_count * block) % block < own_rows)[:, None]

    def pair(values):
        upper = values.astype(jnp.bfloat16)
        return upper, (values - upper.astype(jnp.float32)).astype(jnp.bfloat16)

    basis = start_basis
    ortho = start_basis
    for round_index in range(2):
        basis_high, basis_low = pair(basis)
        both = jnp.dot(
            gathered, jnp.concatenate([basis_high, basis_low], axis=1), preferred_element_type=jnp.float32
        ).reshape(shard_count, 2, block, 2 * rank)
        product = both[:, 0, :, :rank] + both[:, 0, :, rank:] + both[:, 1, :, :rank]
        factor = jnp.where(is_total_row, product.reshape(shard_count * block, rank), 0.0)
        gram = jnp.dot(factor.T, factor, precision=highest)
        lower_factor = jnp.linalg.cholesky(gram)
        ortho = jax.scipy.linalg.solve_triangular(lower_factor, factor.T, lower=True).T
        ortho_high, ortho_low = pair(ortho.reshape(shard_count, 1, block, rank))
        weights = jnp.concatenate(
            [
                jnp.concatenate([ortho_high, ortho_high], axis=1),
                jnp.concatenate([ortho_low, jnp.zeros_like(ortho_low)], axis=1),
            ],
            axis=3,
        ).reshape(shard_count * 2 * block, 2 * rank)
        terms = lax.dot_general(
            gathered, weights, (((0,), (0,)), ((), ())), preferred_element_type=jnp.float32
        )
        basis = (terms[:, :rank] + terms[:, rank:]) / group_count
    own_ortho = lax.dynamic_slice_in_dim(ortho, lax.axis_index("shard") * block, own_rows, axis=0)
    approx = jnp.dot(own_ortho, basis.T, precision=highest)
    new_error = (corrected - approx)[None, :, :]
    new_momentum = momentum_decay * momentum + approx
    new_bias_momentum = momentum_decay * bias_momentum + all_sums / group_count
    new_weight = (weight.astype(jnp.float32) - learn_rate * new_momentum).astype(jnp.bfloat16)
    projected = jnp.dot(
        next_inputs,
        lax.all_gather(new_weight, "shard", axis=0, tiled=True),
        preferred_element_type=jnp.float32,
    )
    return (projected.astype(jnp.bfloat16), new_error, new_momentum, new_bias_momentum)


def split_grp(mesh):
    devices = mesh.devices
    x_count = len({device.coords[0] for device in devices[:, 0]})
    shape = (x_count, devices.shape[0] // x_count, devices.shape[1])
    return Mesh(devices.reshape(shape), ("gx", "gz", "shard"))


def solution(mesh):
    grp = ("gx", "gz")
    placed = (
        P((*grp, "shard"), None),
        P((*grp, "shard"), None),
        P("shard", None),
        P(grp, "shard", None),
        P("shard", None),
        P(),
        P(),
        P((*grp, "shard"), None),
    )
    return jax.shard_map(
        shards,
        mesh=split_grp(mesh),
        in_specs=placed,
        out_specs=(P((*grp, "shard"), None), P(grp, "shard", None), P("shard", None), P()),
        check_vma=False,
    )
```

```python
import jax
import jax.numpy as jnp
from jax import lax
from jax.sharding import Mesh, PartitionSpec as P

momentum_decay = 0.9
learn_rate = 0.1


def shards(
    layer_inputs, cotangents, weight, error_state, momentum, bias_momentum, start_basis, next_inputs
):
    highest = lax.Precision.HIGHEST
    high = lax.Precision.HIGH
    group_count = lax.axis_size("gx") * lax.axis_size("gz")
    shard_count = lax.axis_size("shard")
    gradient = lax.psum_scatter(
        lax.dot_general(
            layer_inputs, cotangents, (((0,), (0,)), ((), ())), preferred_element_type=jnp.float32
        ).astype(jnp.bfloat16),
        "shard",
        scatter_dimension=0,
        tiled=True,
    ).astype(jnp.float32)
    column_sums = jnp.sum(cotangents, axis=0, dtype=jnp.float32)
    corrected = gradient + error_state[0]
    own_rows = corrected.shape[0]
    block = own_rows + 24
    padding = jnp.zeros((block - own_rows - 1, corrected.shape[1]), jnp.float32)
    z_summed = lax.psum(jnp.concatenate([corrected, column_sums[None, :], padding], axis=0), "gz")
    piece = lax.psum_scatter(z_summed, "gx", scatter_dimension=0, tiled=True)
    extended = lax.all_gather(piece, ("shard", "gx"), axis=0, tiled=True)
    all_sums = jnp.sum(extended.reshape(shard_count, block, -1)[:, own_rows], axis=0)
    is_total_row = (jnp.arange(shard_count * block) % block < own_rows)[:, None]
    basis = start_basis
    ortho = start_basis
    for round_index in range(2):
        factor = jnp.where(is_total_row, jnp.dot(extended, basis, precision=high), 0.0)
        gram = jnp.dot(factor.T, factor, precision=highest)
        lower_factor = jnp.linalg.cholesky(gram)
        ortho = jax.scipy.linalg.solve_triangular(lower_factor, factor.T, lower=True).T
        basis = (
            lax.dot_general(extended, ortho, (((0,), (0,)), ((), ())), precision=high)
            / group_count
        )
    own_ortho = lax.dynamic_slice_in_dim(ortho, lax.axis_index("shard") * block, own_rows, axis=0)
    approx = jnp.dot(own_ortho, basis.T, precision=highest)
    new_error = (corrected - approx)[None, :, :]
    new_momentum = momentum_decay * momentum + approx
    new_bias_momentum = momentum_decay * bias_momentum + all_sums / group_count
    new_weight = (weight.astype(jnp.float32) - learn_rate * new_momentum).astype(jnp.bfloat16)
    projected = jnp.dot(
        next_inputs,
        lax.all_gather(new_weight, "shard", axis=0, tiled=True),
        preferred_element_type=jnp.float32,
    )
    return (projected.astype(jnp.bfloat16), new_error, new_momentum, new_bias_momentum)


def split_grp(mesh):
    devices = mesh.devices
    x_count = len({device.coords[0] for device in devices[:, 0]})
    shape = (x_count, devices.shape[0] // x_count, devices.shape[1])
    return Mesh(devices.reshape(shape), ("gx", "gz", "shard"))


def solution(mesh):
    grp = ("gx", "gz")
    placed = (
        P((*grp, "shard"), None),
        P((*grp, "shard"), None),
        P("shard", None),
        P(grp, "shard", None),
        P("shard", None),
        P(),
        P(),
        P((*grp, "shard"), None),
    )
    return jax.shard_map(
        shards,
        mesh=split_grp(mesh),
        in_specs=placed,
        out_specs=(P((*grp, "shard"), None), P(grp, "shard", None), P("shard", None), P()),
        check_vma=False,
    )
```

```python
import jax
import jax.numpy as jnp
from jax import lax
from jax.sharding import Mesh, PartitionSpec as P

momentum_decay = 0.9
learn_rate = 0.1


def shards(
    layer_inputs, cotangents, weight, error_state, momentum, bias_momentum, start_basis, next_inputs
):
    highest = lax.Precision.HIGHEST
    high = lax.Precision.HIGH
    group_count = lax.axis_size("gx") * lax.axis_size("gz")
    shard_count = lax.axis_size("shard")
    gradient = lax.psum_scatter(
        lax.dot_general(
            layer_inputs, cotangents, (((0,), (0,)), ((), ())), preferred_element_type=jnp.float32
        ).astype(jnp.bfloat16),
        "shard",
        scatter_dimension=0,
        tiled=True,
    ).astype(jnp.float32)
    column_sums = jnp.sum(cotangents, axis=0, dtype=jnp.float32)
    corrected = gradient + error_state[0]
    own_rows = corrected.shape[0]
    block = own_rows + 24
    padding = jnp.zeros((block - own_rows - 1, corrected.shape[1]), jnp.float32)
    x_piece = lax.psum_scatter(
        jnp.concatenate([corrected, column_sums[None, :], padding], axis=0),
        "gx",
        scatter_dimension=0,
        tiled=True,
    )
    piece = jnp.sum(lax.all_gather(x_piece, "gz", axis=0), axis=0)
    extended = lax.all_gather(piece, ("shard", "gx"), axis=0, tiled=True)
    all_sums = jnp.sum(extended.reshape(shard_count, block, -1)[:, own_rows], axis=0)
    is_total_row = (jnp.arange(shard_count * block) % block < own_rows)[:, None]
    basis = start_basis
    ortho = start_basis
    for round_index in range(2):
        factor = jnp.where(is_total_row, jnp.dot(extended, basis, precision=high), 0.0)
        gram = jnp.dot(factor.T, factor, precision=highest)
        lower_factor = jnp.linalg.cholesky(gram)
        ortho = jax.scipy.linalg.solve_triangular(lower_factor, factor.T, lower=True).T
        basis = (
            lax.dot_general(extended, ortho, (((0,), (0,)), ((), ())), precision=high)
            / group_count
        )
    own_ortho = lax.dynamic_slice_in_dim(ortho, lax.axis_index("shard") * block, own_rows, axis=0)
    approx = jnp.dot(own_ortho, basis.T, precision=highest)
    new_error = (corrected - approx)[None, :, :]
    new_momentum = momentum_decay * momentum + approx
    new_bias_momentum = momentum_decay * bias_momentum + all_sums / group_count
    new_weight = (weight.astype(jnp.float32) - learn_rate * new_momentum).astype(jnp.bfloat16)
    projected = jnp.dot(
        next_inputs,
        lax.all_gather(new_weight, "shard", axis=0, tiled=True),
        preferred_element_type=jnp.float32,
    )
    return (projected.astype(jnp.bfloat16), new_error, new_momentum, new_bias_momentum)


def split_grp(mesh):
    devices = mesh.devices
    x_count = len({device.coords[0] for device in devices[:, 0]})
    shape = (x_count, devices.shape[0] // x_count, devices.shape[1])
    return Mesh(devices.reshape(shape), ("gx", "gz", "shard"))


def solution(mesh):
    grp = ("gx", "gz")
    placed = (
        P((*grp, "shard"), None),
        P((*grp, "shard"), None),
        P("shard", None),
        P(grp, "shard", None),
        P("shard", None),
        P(),
        P(),
        P((*grp, "shard"), None),
    )
    return jax.shard_map(
        shards,
        mesh=split_grp(mesh),
        in_specs=placed,
        out_specs=(P((*grp, "shard"), None), P(grp, "shard", None), P("shard", None), P()),
        check_vma=False,
    )
```
